512 devices in a mesh: pair: 64 (over z_hi, y, x), win: 8 (over z_lo, core).
Axes of the slice: x: 4, y: 8, z: 8 (z_hi: 2, z_lo: 4; z = z_hi * 4 + z_lo), core: 2. Of those that a mesh axis runs over, the one named last changes fastest.
Arguments:
- spectra: bfloat16 [32, 1024, 3, 8192], P('win', 'pair'), may hold values from -6 to 6
- pair_first: int32 [64, 64], P('pair'), may hold values from 0 to 1023, as said below
- pair_second: int32 [64, 64], P('pair'), may hold values from 0 to 1023, as said below
- pair_count: int32 [64], P('pair'), may hold values from 16 to 64, as said below
Outputs:
- stacks: float32 [4096, 9, 256], P(('pair', 'win'))
The draws below stay inside these ranges and needn't reach their ends.
Inputs may be any that keep to these rules, and one draw needn't show every extreme that they name: Stations are numbered block by block, 16 to a block. In block b every pair_first lies in block b; pair_second lies in block b and differs from pair_first, or in block b + 1 among its first 8 stations; the last block has no pairs into a further block. Slots past pair_count hold pairs of the same kind. `pair_second`: see pair_first. `pair_count`: some block is full in every draw.
All inputs are finite; a program needn't handle non-finite values.
Results may differ from the reference program's by a relative error of at most 0.0039.
Values may be sent and summed in bfloat16 or wider, within the bound.
No kernel may reach another device: no remote copies, remote signals or barrier semaphores. Data moves between devices by JAX's collectives and lax.ppermute only.
A program may use at most 128 MiB of HBM per device.

```python
import jax
import jax.numpy as jnp
from jax import lax

F = 4096
LAGS = 256
S_DEV = 16
W_DEV = 4
P_CAP = 64
BLOCKS = 64
STATIONS = 1024
WINDOWS = 32
PAIRS = 4096
N_WIN = 8


def pair_lists(key):
    keys_all = [jax.random.fold_in(key, 11 + offset) for offset in range(4)]
    block_ids = jnp.arange(BLOCKS, dtype=jnp.int32)[:, None]
    first_local = jax.random.randint(keys_all[0], (BLOCKS, P_CAP), 0, S_DEV)
    crossing = jax.random.randint(keys_all[1], (BLOCKS, P_CAP), 0, 2) * (block_ids < BLOCKS - 1).astype(jnp.int32)
    far_local = jax.random.randint(keys_all[2], (BLOCKS, P_CAP), 0, S_DEV // 2)
    near_step = jax.random.randint(keys_all[3], (BLOCKS, P_CAP), 1, S_DEV)
    near_local = (first_local + near_step) % S_DEV
    second_global = jnp.where(crossing == 1, (block_ids + 1) * S_DEV + far_local, block_ids * S_DEV + near_local)
    return ((block_ids * S_DEV + first_local).astype(jnp.int32), second_global.astype(jnp.int32))


def draw_pair_first(key, part):
    return pair_lists(key)[0]


def draw_pair_second(key, part):
    return pair_lists(key)[1]


def draw_pair_count(key, part):
    counts = jax.random.randint(jax.random.fold_in(key, 31), (BLOCKS,), P_CAP // 4, P_CAP + 1)
    full_block = jax.random.randint(jax.random.fold_in(key, 37), (), 0, BLOCKS)
    return jnp.where(jnp.arange(BLOCKS, dtype=jnp.int32) == full_block, P_CAP, counts).astype(jnp.int32)


def steps_of(key, shape, cuts, least, high):
    factor_of = 1.0
    for dim, blocks in cuts:
        draws = jax.random.uniform(jax.random.fold_in(jax.random.fold_in(key, 6), dim), (blocks,), jnp.float32, least / len(cuts), high / len(cuts))
        factor_of = factor_of * jnp.repeat(jnp.exp(draws), shape[dim] // blocks).reshape((-1,) + (1,) * (len(shape) - 1 - dim))
    return factor_of


def scatter_about(own_key, shape, spread, bound, cuts=(), held_as=jnp.bfloat16):
    drawn = spread * jax.random.normal(own_key, shape, jnp.float32)
    if cuts:
        drawn = drawn * steps_of(own_key, shape, cuts, -0.22, 0.18)
    return jnp.clip(drawn, -bound, bound).astype(held_as)


def setup_inputs(seed: int = 0) -> dict:
    key_list = jax.random.split(jax.random.key(seed), 5)
    return {
        "spectra": scatter_about(key_list[0], (WINDOWS, STATIONS, 3, 2 * F), 1.0, 6.0, ((0, 8), (1, 64))),
        "pair_first": draw_pair_first(jax.random.fold_in(key_list[4], 71), 0),
        "pair_second": draw_pair_second(jax.random.fold_in(key_list[4], 71), 0),
        "pair_count": draw_pair_count(jax.random.fold_in(key_list[4], 71), 0),
    }


def lag_table(bins_count, lags_count, windows_all):
    bin_index = jnp.arange(bins_count, dtype=jnp.int32)
    lag_index = jnp.arange(lags_count, dtype=jnp.int32) - lags_count // 2
    phase_index = jnp.mod(bin_index[:, None] * lag_index[None, :], 2 * bins_count)
    angles = phase_index.astype(jnp.float32) * (jnp.pi / bins_count)
    window_taper = 0.5 + 0.5 * jnp.cos(lag_index.astype(jnp.float32) * (2.0 * jnp.pi / lags_count))
    norm_scale = 1.0 / jnp.sqrt(jnp.float32(2 * windows_all * bins_count))
    weights = jnp.concatenate([jnp.cos(angles), -jnp.sin(angles)], 0) * (window_taper * norm_scale)[None, :]
    return weights.astype(jnp.bfloat16)

def cross_block(stations_all, first_local, second_local, valid_mask, lag_weights):
    left_rows = jnp.take(stations_all, first_local, axis=1).astype(jnp.float32)
    right_rows = jnp.take(stations_all, second_local, axis=1).astype(jnp.float32)
    bins_count = stations_all.shape[-1] // 2
    left_real, left_imag = (left_rows[..., :bins_count], left_rows[..., bins_count:])
    right_real, right_imag = (right_rows[..., :bins_count], right_rows[..., bins_count:])
    cross_real = lax.optimization_barrier(jnp.sum(left_real[:, :, :, None] * right_real[:, :, None] + left_imag[:, :, :, None] * right_imag[:, :, None], axis=0))
    cross_imag = lax.optimization_barrier(jnp.sum(left_imag[:, :, :, None] * right_real[:, :, None] - left_real[:, :, :, None] * right_imag[:, :, None], axis=0))
    cross_rows = jnp.concatenate([cross_real, cross_imag], -1) * valid_mask[:, None, None, None]
    count_rows = cross_rows.shape[0]
    cross_rows = cross_rows.reshape(count_rows * 9, 2 * bins_count).astype(jnp.bfloat16)
    result = jnp.dot(cross_rows, lag_weights, preferred_element_type=jnp.float32)
    return result.reshape(count_rows, 9, lag_weights.shape[1])

def reference(spectra, pair_first, pair_second, pair_count):
    lag_weights = lag_table(F, LAGS, WINDOWS)
    slot_index = jnp.arange(P_CAP, dtype=jnp.int32)
    valid_mask = (slot_index[None, :] < pair_count[:, None]).astype(jnp.float32)

    def one_block(inputs):
        first_ids, second_ids, block_mask = inputs
        stack_sum = jnp.zeros((P_CAP, 9, LAGS), jnp.float32)
        for group_index in range(N_WIN):
            window_group = spectra[group_index * W_DEV:(group_index + 1) * W_DEV]
            stack_sum = stack_sum + cross_block(window_group, first_ids, second_ids, block_mask, lag_weights)
        return stack_sum
    stacked = lax.map(one_block, (pair_first, pair_second, valid_mask))
    return stacked.reshape(PAIRS, 9, LAGS)
```

```python
import jax
import jax.numpy as jnp
from jax import lax
from jax.experimental import pallas as pl
from jax.experimental.pallas import tpu as pltpu
from jax.sharding import PartitionSpec as P

LAGS = 256
CHUNK = 512


def shifted(shard, axis, by):
    peers = lax.axis_size(axis)
    pairs = [(i, i + by) for i in range(peers) if 0 <= i + by < peers]
    return lax.ppermute(shard, axis, pairs)


def lag_table(bins_count, lags_count, windows_all):
    bin_index = jnp.arange(bins_count, dtype=jnp.int32)
    lag_index = jnp.arange(lags_count, dtype=jnp.int32) - lags_count // 2
    phase_index = jnp.mod(bin_index[:, None] * lag_index[None, :], 2 * bins_count)
    angles = phase_index.astype(jnp.float32) * (jnp.pi / bins_count)
    window_taper = 0.5 + 0.5 * jnp.cos(lag_index.astype(jnp.float32) * (2.0 * jnp.pi / lags_count))
    norm_scale = 1.0 / jnp.sqrt(jnp.float32(2 * windows_all * bins_count))
    weights = (
        jnp.concatenate([jnp.cos(angles), -jnp.sin(angles)], 0)
        * (window_taper * norm_scale)[None, :]
    )
    return weights.astype(jnp.bfloat16)


def stack_kernel(n_win, n_comp, owners, lr_ref, li_ref, rr_ref, ri_ref, valid_ref, wr_ref, wi_ref, out_ref):
    @pl.when(pl.program_id(0) == 0)
    def _():
        out_ref[...] = jnp.zeros_like(out_ref)

    valid = valid_ref[...]
    wr = wr_ref[...]
    wi = wi_ref[...]
    slots = lr_ref.shape[1]
    for a in range(n_comp):
        lr = [lr_ref[w * n_comp + a].astype(jnp.float32) for w in range(n_win)]
        li = [li_ref[w * n_comp + a].astype(jnp.float32) for w in range(n_win)]
        for c in range(n_comp):
            re = None
            im = None
            for w in range(n_win):
                rr = rr_ref[w * n_comp + c].astype(jnp.float32)
                ri = ri_ref[w * n_comp + c].astype(jnp.float32)
                re_w = lr[w] * rr + li[w] * ri
                im_w = li[w] * rr - lr[w] * ri
                re = re_w if re is None else re + re_w
                im = im_w if im is None else im + im_w
            re = (re * valid).astype(jnp.bfloat16)
            im = (im * valid).astype(jnp.bfloat16)
            term = jnp.dot(re, wr, preferred_element_type=jnp.float32)
            term = term + jnp.dot(im, wi, preferred_element_type=jnp.float32)
            ac = a * n_comp + c
            out_ref[:, ac] += term.reshape(owners, slots // owners, term.shape[-1])


def stacks_of(left, right, valid, lag_weights, owners):
    rows, slots, twice = left.shape
    bins_count = twice // 2
    n_comp = 3
    n_win = rows // n_comp
    steps = bins_count // CHUNK
    lags = lag_weights.shape[1]
    spec_re = pl.BlockSpec((rows, slots, CHUNK), lambda k: (0, 0, k))
    spec_im = pl.BlockSpec((rows, slots, CHUNK), lambda k: (0, 0, k + steps))
    kernel = lambda *refs: stack_kernel(n_win, n_comp, owners, *refs)
    flops = 2 * slots * 9 * twice * lags + 8 * slots * 9 * bins_count * n_win
    bytes_accessed = 2 * left.size * 2 + lag_weights.size * 2 + owners * 9 * slots * lags * 4
    return pl.pallas_call(
        kernel,
        grid=(steps,),
        in_specs=[
            spec_re,
            spec_im,
            spec_re,
            spec_im,
            pl.BlockSpec((slots, 1), lambda k: (0, 0)),
            pl.BlockSpec((CHUNK, lags), lambda k: (k, 0)),
            pl.BlockSpec((CHUNK, lags), lambda k: (k + steps, 0)),
        ],
        out_specs=pl.BlockSpec((owners, 9, slots // owners, lags), lambda k: (0, 0, 0, 0)),
        out_shape=jax.ShapeDtypeStruct((owners, 9, slots // owners, lags), jnp.float32),
        compiler_params=pltpu.CompilerParams(
            dimension_semantics=("arbitrary",), vmem_limit_bytes=48 * 1024 * 1024
        ),
        cost_estimate=pl.CostEstimate(
            flops=flops, transcendentals=0, bytes_accessed=bytes_accessed
        ),
    )(left, left, right, right, valid, lag_weights, lag_weights)


def per_device(spectra, pair_first, pair_second, pair_count):
    block_size = spectra.shape[1]
    owners = lax.axis_size("win")
    block_index = lax.axis_index("pair")
    next_stations = shifted(spectra[:, : block_size // 2], "pair", -1)
    windows_all = spectra.shape[0] * owners
    lag_weights = lag_table(spectra.shape[-1] // 2, LAGS, windows_all)
    block_start = block_index * block_size
    first_local = pair_first[0] - block_start
    second_local = pair_second[0] - block_start
    slots = first_local.shape[0]
    slot_index = jnp.arange(slots, dtype=jnp.int32)
    valid = (slot_index < pair_count[0]).astype(jnp.float32)[:, None]

    table = jnp.concatenate([spectra, next_stations], axis=1)
    left = jnp.take(spectra, first_local, axis=1, mode="clip")
    right = jnp.take(table, second_local, axis=1, mode="clip")
    n_w, _, n_c, twice = spectra.shape
    left = jnp.transpose(left, (0, 2, 1, 3)).reshape(n_w * n_c, slots, twice)
    right = jnp.transpose(right, (0, 2, 1, 3)).reshape(n_w * n_c, slots, twice)

    partial = stacks_of(left, right, valid, lag_weights, owners)
    received = lax.all_to_all(partial, "win", 0, 0, tiled=True)
    mine = jnp.sum(received, axis=0)
    return jnp.transpose(mine, (1, 0, 2))


def solution(mesh):
    return jax.shard_map(
        per_device,
        mesh=mesh,
        in_specs=(P("win", "pair", None, None), P("pair", None), P("pair", None), P("pair")),
        out_specs=P(("pair", "win"), None, None),
        check_vma=False,
    )
```

```python
import jax
import jax.numpy as jnp
from jax import lax
from jax.experimental import pallas as pl
from jax.experimental.pallas import tpu as pltpu
from jax.sharding import PartitionSpec as P

LAGS = 256
CHUNK = 512


def shifted(shard, axis, by):
    peers = lax.axis_size(axis)
    pairs = [(i, i + by) for i in range(peers) if 0 <= i + by < peers]
    return lax.ppermute(shard, axis, pairs)


def lag_table(bins_count, lags_count, windows_all):
    bin_index = jnp.arange(bins_count, dtype=jnp.int32)
    lag_index = jnp.arange(lags_count, dtype=jnp.int32) - lags_count // 2
    phase_index = jnp.mod(bin_index[:, None] * lag_index[None, :], 2 * bins_count)
    angles = phase_index.astype(jnp.float32) * (jnp.pi / bins_count)
    window_taper = 0.5 + 0.5 * jnp.cos(lag_index.astype(jnp.float32) * (2.0 * jnp.pi / lags_count))
    norm_scale = 1.0 / jnp.sqrt(jnp.float32(2 * windows_all * bins_count))
    weights = (
        jnp.concatenate([jnp.cos(angles), -jnp.sin(angles)], 0)
        * (window_taper * norm_scale)[None, :]
    )
    return weights.astype(jnp.bfloat16)


def stack_kernel(n_win, n_comp, owners, lr_ref, li_ref, rr_ref, ri_ref, valid_ref, wr_ref, wi_ref, out_ref):
    @pl.when(pl.program_id(0) == 0)
    def _():
        out_ref[...] = jnp.zeros_like(out_ref)

    valid = valid_ref[...]
    wr = wr_ref[...]
    wi = wi_ref[...]
    slots = lr_ref.shape[1]
    for a in range(n_comp):
        lr = [lr_ref[w * n_comp + a].astype(jnp.float32) for w in range(n_win)]
        li = [li_ref[w * n_comp + a].astype(jnp.float32) for w in range(n_win)]
        for c in range(n_comp):
            re = None
            im = None
            for w in range(n_win):
                rr = rr_ref[w * n_comp + c].astype(jnp.float32)
                ri = ri_ref[w * n_comp + c].astype(jnp.float32)
                re_w = lr[w] * rr + li[w] * ri
                im_w = li[w] * rr - lr[w] * ri
                re = re_w if re is None else re + re_w
                im = im_w if im is None else im + im_w
            re = (re * valid).astype(jnp.bfloat16)
            im = (im * valid).astype(jnp.bfloat16)
            term = jnp.dot(re, wr, preferred_element_type=jnp.float32)
            term = term + jnp.dot(im, wi, preferred_element_type=jnp.float32)
            ac = a * n_comp + c
            out_ref[:, ac] += term.reshape(owners, slots // owners, term.shape[-1])


def stacks_of(left, right, valid, lag_weights, owners):
    rows, slots, twice = left.shape
    bins_count = twice // 2
    n_comp = 3
    n_win = rows // n_comp
    steps = bins_count // CHUNK
    lags = lag_weights.shape[1]
    spec_re = pl.BlockSpec((rows, slots, CHUNK), lambda k: (0, 0, k))
    spec_im = pl.BlockSpec((rows, slots, CHUNK), lambda k: (0, 0, k + steps))
    kernel = lambda *refs: stack_kernel(n_win, n_comp, owners, *refs)
    flops = 2 * slots * 9 * twice * lags + 8 * slots * 9 * bins_count * n_win
    bytes_accessed = 2 * left.size * 2 + lag_weights.size * 2 + owners * 9 * slots * lags * 4
    return pl.pallas_call(
        kernel,
        grid=(steps,),
        in_specs=[
            spec_re,
            spec_im,
            spec_re,
            spec_im,
            pl.BlockSpec((slots, 1), lambda k: (0, 0)),
            pl.BlockSpec((CHUNK, lags), lambda k: (k, 0)),
            pl.BlockSpec((CHUNK, lags), lambda k: (k + steps, 0)),
        ],
        out_specs=pl.BlockSpec((owners, 9, slots // owners, lags), lambda k: (0, 0, 0, 0)),
        out_shape=jax.ShapeDtypeStruct((owners, 9, slots // owners, lags), jnp.float32),
        compiler_params=pltpu.CompilerParams(
            dimension_semantics=("arbitrary",), vmem_limit_bytes=48 * 1024 * 1024
        ),
        cost_estimate=pl.CostEstimate(
            flops=flops, transcendentals=0, bytes_accessed=bytes_accessed
        ),
    )(left, left, right, right, valid, lag_weights, lag_weights)


def per_device(spectra, pair_first, pair_second, pair_count):
    block_size = spectra.shape[1]
    owners = lax.axis_size("win")
    block_index = lax.axis_index("pair")
    next_stations = shifted(spectra[:, : block_size // 2], "pair", -1)
    windows_all = spectra.shape[0] * owners
    lag_weights = lag_table(spectra.shape[-1] // 2, LAGS, windows_all)
    block_start = block_index * block_size
    first_local = pair_first[0] - block_start
    second_local = pair_second[0] - block_start
    slots = first_local.shape[0]
    slot_index = jnp.arange(slots, dtype=jnp.int32)
    valid = (slot_index < pair_count[0]).astype(jnp.float32)[:, None]

    n_w, _, n_c, twice = spectra.shape
    own_rows = jnp.transpose(spectra, (0, 2, 1, 3)).reshape(n_w * n_c, block_size, twice)
    next_rows = jnp.transpose(next_stations, (0, 2, 1, 3)).reshape(n_w * n_c, block_size // 2, twice)
    table = jnp.concatenate([own_rows, next_rows], axis=1)
    own_cols = jnp.arange(block_size, dtype=jnp.int32)
    table_cols = jnp.arange(table.shape[1], dtype=jnp.int32)
    pick_first = (first_local[:, None] == own_cols[None, :]).astype(jnp.bfloat16)
    pick_second = (second_local[:, None] == table_cols[None, :]).astype(jnp.bfloat16)
    left = jnp.einsum("ps,xsk->xpk", pick_first, own_rows, preferred_element_type=jnp.bfloat16)
    right = jnp.einsum("ps,xsk->xpk", pick_second, table, preferred_element_type=jnp.bfloat16)

    partial = stacks_of(left, right, valid, lag_weights, owners)
    received = lax.all_to_all(partial, "win", 0, 0, tiled=True)
    mine = jnp.sum(received, axis=0)
    return jnp.transpose(mine, (1, 0, 2))


def solution(mesh):
    return jax.shard_map(
        per_device,
        mesh=mesh,
        in_specs=(P("win", "pair", None, None), P("pair", None), P("pair", None), P("pair")),
        out_specs=P(("pair", "win"), None, None),
        check_vma=False,
    )
```

```python
import jax
import jax.numpy as jnp
from jax import lax
from jax.experimental import pallas as pl
from jax.experimental.pallas import tpu as pltpu
from jax.sharding import PartitionSpec as P

LAGS = 256
CHUNK = 512
CHUNKS = 4


def shifted(shard, axis, by):
    peers = lax.axis_size(axis)
    pairs = [(i, i + by) for i in range(peers) if 0 <= i + by < peers]
    return lax.ppermute(shard, axis, pairs)


def lag_table(bins_count, lags_count, windows_all):
    bin_index = jnp.arange(bins_count, dtype=jnp.int32)
    lag_index = jnp.arange(lags_count, dtype=jnp.int32) - lags_count // 2
    phase_index = jnp.mod(bin_index[:, None] * lag_index[None, :], 2 * bins_count)
    angles = phase_index.astype(jnp.float32) * (jnp.pi / bins_count)
    window_taper = 0.5 + 0.5 * jnp.cos(lag_index.astype(jnp.float32) * (2.0 * jnp.pi / lags_count))
    norm_scale = 1.0 / jnp.sqrt(jnp.float32(2 * windows_all * bins_count))
    weights = (
        jnp.concatenate([jnp.cos(angles), -jnp.sin(angles)], 0)
        * (window_taper * norm_scale)[None, :]
    )
    return weights.astype(jnp.bfloat16)


def stack_kernel(n_win, n_comp, owners, lr_ref, li_ref, rr_ref, ri_ref, valid_ref, wr_ref, wi_ref, out_ref):
    @pl.when(pl.program_id(0) == 0)
    def _():
        out_ref[...] = jnp.zeros_like(out_ref)

    valid = valid_ref[...]
    slots = lr_ref.shape[1]

    def one_pair(ac, carry):
        a = ac // n_comp
        c = ac % n_comp
        re = None
        im = None
        for w in range(n_win):
            lr = lr_ref[w * n_comp + a].astype(jnp.float32)
            li = li_ref[w * n_comp + a].astype(jnp.float32)
            rr = rr_ref[w * n_comp + c].astype(jnp.float32)
            ri = ri_ref[w * n_comp + c].astype(jnp.float32)
            re_w = lr * rr + li * ri
            im_w = li * rr - lr * ri
            re = re_w if re is None else re + re_w
            im = im_w if im is None else im + im_w
        re = (re * valid).astype(jnp.bfloat16)
        im = (im * valid).astype(jnp.bfloat16)
        term = jnp.dot(re, wr_ref[...], preferred_element_type=jnp.float32)
        term = term + jnp.dot(im, wi_ref[...], preferred_element_type=jnp.float32)
        out_ref[ac] += term.reshape(owners, slots // owners, term.shape[-1])
        return carry

    lax.fori_loop(0, n_comp * n_comp, one_pair, 0)


def stacks_of(left, right, valid, lag_weights, owners, chunk, chunks):
    rows, slots, twice = left.shape
    bins_count = twice // 2
    n_comp = 3
    n_win = rows // n_comp
    steps = bins_count // CHUNK
    part = steps // chunks
    base = chunk * part
    lags = lag_weights.shape[1]
    left_re = pl.BlockSpec((rows, slots, CHUNK), lambda k: (0, 0, base + k))
    left_im = pl.BlockSpec((rows, slots, CHUNK), lambda k: (0, 0, base + k + steps))
    right_re = pl.BlockSpec((rows, slots, CHUNK), lambda k: (0, 0, k))
    right_im = pl.BlockSpec((rows, slots, CHUNK), lambda k: (0, 0, k + part))
    kernel = lambda *refs: stack_kernel(n_win, n_comp, owners, *refs)
    flops = (2 * slots * 9 * twice * lags + 8 * slots * 9 * bins_count * n_win) // chunks
    bytes_accessed = (2 * left.size * 2 + lag_weights.size * 2) // chunks + owners * 9 * slots * lags * 4
    return pl.pallas_call(
        kernel,
        grid=(part,),
        in_specs=[
            left_re,
            left_im,
            right_re,
            right_im,
            pl.BlockSpec((slots, 1), lambda k: (0, 0)),
            pl.BlockSpec((CHUNK, lags), lambda k: (base + k, 0)),
            pl.BlockSpec((CHUNK, lags), lambda k: (base + k + steps, 0)),
        ],
        out_specs=pl.BlockSpec((9, owners, slots // owners, lags), lambda k: (0, 0, 0, 0)),
        out_shape=jax.ShapeDtypeStruct((9, owners, slots // owners, lags), jnp.float32),
        compiler_params=pltpu.CompilerParams(
            dimension_semantics=("arbitrary",), vmem_limit_bytes=48 * 1024 * 1024
        ),
        cost_estimate=pl.CostEstimate(
            flops=flops, transcendentals=0, bytes_accessed=bytes_accessed
        ),
    )(left, left, right, right, valid, lag_weights, lag_weights)


def per_device(spectra, pair_first, pair_second, pair_count):
    n_w, block_size, n_c, twice = spectra.shape
    bins_count = twice // 2
    owners = lax.axis_size("win")
    block_index = lax.axis_index("pair")
    windows_all = n_w * owners
    chunks = CHUNKS
    width = bins_count // chunks
    halves = spectra[:, : block_size // 2].reshape(n_w, block_size // 2, n_c, 2, chunks, width)
    sent = [shifted(halves[:, :, :, :, q], "pair", -1) for q in range(chunks)]
    lag_weights = lag_table(bins_count, LAGS, windows_all)
    block_start = block_index * block_size
    first_local = pair_first[0] - block_start
    second_local = pair_second[0] - block_start
    slots = first_local.shape[0]
    slot_index = jnp.arange(slots, dtype=jnp.int32)
    valid = (slot_index < pair_count[0]).astype(jnp.float32)[:, None]

    own_rows = jnp.transpose(spectra, (0, 2, 1, 3)).reshape(n_w * n_c, block_size, twice)
    own_cols = jnp.arange(block_size, dtype=jnp.int32)
    table_cols = jnp.arange(block_size + block_size // 2, dtype=jnp.int32)
    pick_first = (first_local[:, None] == own_cols[None, :]).astype(jnp.bfloat16)
    pick_second = (second_local[:, None] == table_cols[None, :]).astype(jnp.bfloat16)
    left = jnp.einsum("ps,xsk->xpk", pick_first, own_rows, preferred_element_type=jnp.bfloat16)
    own_parts = own_rows.reshape(n_w * n_c, block_size, 2, chunks, width)

    partial = None
    for q in range(chunks):
        next_rows = jnp.transpose(sent[q], (0, 2, 1, 3, 4)).reshape(
            n_w * n_c, block_size // 2, 2 * width
        )
        own_q = own_parts[:, :, :, q].reshape(n_w * n_c, block_size, 2 * width)
        table = jnp.concatenate([own_q, next_rows], axis=1)
        right = jnp.einsum("ps,xsk->xpk", pick_second, table, preferred_element_type=jnp.bfloat16)
        term = stacks_of(left, right, valid, lag_weights, owners, q, chunks)
        partial = term if partial is None else partial + term
    partial = jnp.transpose(partial, (1, 0, 2, 3))
    received = lax.all_to_all(partial, "win", 0, 0, tiled=True)
    mine = jnp.sum(received, axis=0)
    return jnp.transpose(mine, (1, 0, 2))


def solution(mesh):
    return jax.shard_map(
        per_device,
        mesh=mesh,
        in_specs=(P("win", "pair", None, None), P("pair", None), P("pair", None), P("pair")),
        out_specs=P(("pair", "win"), None, None),
        check_vma=False,
    )
```

```python
import jax
import jax.numpy as jnp
from jax import lax
from jax.experimental import pallas as pl
from jax.experimental.pallas import tpu as pltpu
from jax.sharding import PartitionSpec as P

LAGS = 256
CHUNK = 512
CHUNKS = 2


def shifted(shard, axis, by):
    peers = lax.axis_size(axis)
    pairs = [(i, i + by) for i in range(peers) if 0 <= i + by < peers]
    return lax.ppermute(shard, axis, pairs)


def lag_table(bins_count, lags_count, windows_all):
    bin_index = jnp.arange(bins_count, dtype=jnp.int32)
    lag_index = jnp.arange(lags_count, dtype=jnp.int32) - lags_count // 2
    phase_index = jnp.mod(bin_index[:, None] * lag_index[None, :], 2 * bins_count)
    angles = phase_index.astype(jnp.float32) * (jnp.pi / bins_count)
    window_taper = 0.5 + 0.5 * jnp.cos(lag_index.astype(jnp.float32) * (2.0 * jnp.pi / lags_count))
    norm_scale = 1.0 / jnp.sqrt(jnp.float32(2 * windows_all * bins_count))
    weights = (
        jnp.concatenate([jnp.cos(angles), -jnp.sin(angles)], 0)
        * (window_taper * norm_scale)[None, :]
    )
    return weights.astype(jnp.bfloat16)


def stack_kernel(n_win, n_comp, owners, lr_ref, li_ref, rr_ref, ri_ref, valid_ref, wr_ref, wi_ref, *rest):
    if len(rest) == 2:
        init_ref, out_ref = rest
    else:
        (out_ref,) = rest
        init_ref = None

    @pl.when(pl.program_id(0) == 0)
    def _():
        if init_ref is None:
            out_ref[...] = jnp.zeros_like(out_ref)
        else:
            out_ref[...] = init_ref[...]

    valid = valid_ref[...]
    wr = wr_ref[...]
    wi = wi_ref[...]
    slots = lr_ref.shape[1]
    for a in range(n_comp):
        lr = [lr_ref[w * n_comp + a].astype(jnp.float32) for w in range(n_win)]
        li = [li_ref[w * n_comp + a].astype(jnp.float32) for w in range(n_win)]
        for c in range(n_comp):
            re = None
            im = None
            for w in range(n_win):
                rr = rr_ref[w * n_comp + c].astype(jnp.float32)
                ri = ri_ref[w * n_comp + c].astype(jnp.float32)
                re_w = lr[w] * rr + li[w] * ri
                im_w = li[w] * rr - lr[w] * ri
                re = re_w if re is None else re + re_w
                im = im_w if im is None else im + im_w
            re = (re * valid).astype(jnp.bfloat16)
            im = (im * valid).astype(jnp.bfloat16)
            term = jnp.dot(re, wr, preferred_element_type=jnp.float32)
            term = term + jnp.dot(im, wi, preferred_element_type=jnp.float32)
            out_ref[a * n_comp + c] += term.reshape(owners, slots // owners, term.shape[-1])


def stacks_of(left, right, valid, lag_weights, owners, chunk, chunks, init=None):
    rows, slots, twice = left.shape
    bins_count = twice // 2
    n_comp = 3
    n_win = rows // n_comp
    steps = bins_count // CHUNK
    part = steps // chunks
    base = chunk * part
    lags = lag_weights.shape[1]
    left_re = pl.BlockSpec((rows, slots, CHUNK), lambda k: (0, 0, base + k))
    left_im = pl.BlockSpec((rows, slots, CHUNK), lambda k: (0, 0, base + k + steps))
    right_re = pl.BlockSpec((rows, slots, CHUNK), lambda k: (0, 0, k))
    right_im = pl.BlockSpec((rows, slots, CHUNK), lambda k: (0, 0, k + part))
    kernel = lambda *refs: stack_kernel(n_win, n_comp, owners, *refs)
    out_block = pl.BlockSpec((9, owners, slots // owners, lags), lambda k: (0, 0, 0, 0))
    extra = [] if init is None else [init]
    extra_specs = [] if init is None else [out_block]
    aliases = {} if init is None else {7: 0}
    flops = (2 * slots * 9 * twice * lags + 8 * slots * 9 * bins_count * n_win) // chunks
    bytes_accessed = (2 * left.size * 2 + lag_weights.size * 2) // chunks + owners * 9 * slots * lags * 4
    return pl.pallas_call(
        kernel,
        grid=(part,),
        in_specs=[
            left_re,
            left_im,
            right_re,
            right_im,
            pl.BlockSpec((slots, 1), lambda k: (0, 0)),
            pl.BlockSpec((CHUNK, lags), lambda k: (base + k, 0)),
            pl.BlockSpec((CHUNK, lags), lambda k: (base + k + steps, 0)),
        ]
        + extra_specs,
        out_specs=pl.BlockSpec((9, owners, slots // owners, lags), lambda k: (0, 0, 0, 0)),
        out_shape=jax.ShapeDtypeStruct((9, owners, slots // owners, lags), jnp.float32),
        compiler_params=pltpu.CompilerParams(
            dimension_semantics=("arbitrary",), vmem_limit_bytes=48 * 1024 * 1024
        ),
        cost_estimate=pl.CostEstimate(
            flops=flops, transcendentals=0, bytes_accessed=bytes_accessed
        ),
        input_output_aliases=aliases,
    )(left, left, right, right, valid, lag_weights, lag_weights, *extra)


def per_device(spectra, pair_first, pair_second, pair_count):
    n_w, block_size, n_c, twice = spectra.shape
    bins_count = twice // 2
    owners = lax.axis_size("win")
    block_index = lax.axis_index("pair")
    windows_all = n_w * owners
    chunks = CHUNKS
    width = bins_count // chunks
    halves = spectra[:, : block_size // 2].reshape(n_w, block_size // 2, n_c, 2, chunks, width)
    sent = [shifted(halves[:, :, :, :, q], "pair", -1) for q in range(chunks)]
    lag_weights = lag_table(bins_count, LAGS, windows_all)
    block_start = block_index * block_size
    first_local = pair_first[0] - block_start
    second_local = pair_second[0] - block_start
    slots = first_local.shape[0]
    slot_index = jnp.arange(slots, dtype=jnp.int32)
    valid = (slot_index < pair_count[0]).astype(jnp.float32)[:, None]

    own_rows = jnp.transpose(spectra, (0, 2, 1, 3)).reshape(n_w * n_c, block_size, twice)
    own_cols = jnp.arange(block_size, dtype=jnp.int32)
    table_cols = jnp.arange(block_size + block_size // 2, dtype=jnp.int32)
    pick_first = (first_local[:, None] == own_cols[None, :]).astype(jnp.bfloat16)
    pick_second = (second_local[:, None] == table_cols[None, :]).astype(jnp.bfloat16)
    left = jnp.einsum("ps,xsk->xpk", pick_first, own_rows, preferred_element_type=jnp.bfloat16)
    own_parts = own_rows.reshape(n_w * n_c, block_size, 2, chunks, width)

    partial = None
    for q in range(chunks):
        next_rows = jnp.transpose(sent[q], (0, 2, 1, 3, 4)).reshape(
            n_w * n_c, block_size // 2, 2 * width
        )
        own_q = own_parts[:, :, :, q].reshape(n_w * n_c, block_size, 2 * width)
        table = jnp.concatenate([own_q, next_rows], axis=1)
        picks = pick_second
        if partial is not None:
            picks, partial = lax.optimization_barrier((pick_second, partial))
        right = jnp.einsum("ps,xsk->xpk", picks, table, preferred_element_type=jnp.bfloat16)
        partial = stacks_of(left, right, valid, lag_weights, owners, q, chunks, partial)
    partial = jnp.transpose(partial, (1, 0, 2, 3))
    received = lax.all_to_all(partial, "win", 0, 0, tiled=True)
    mine = jnp.sum(received, axis=0)
    return jnp.transpose(mine, (1, 0, 2))


def solution(mesh):
    return jax.shard_map(
        per_device,
        mesh=mesh,
        in_specs=(P("win", "pair", None, None), P("pair", None), P("pair", None), P("pair")),
        out_specs=P(("pair", "win"), None, None),
        check_vma=False,
    )
```

```python
import jax
import jax.numpy as jnp
from jax import lax
from jax.experimental import pallas as pl
from jax.experimental.pallas import tpu as pltpu
from jax.sharding import PartitionSpec as P

LAGS = 256
CHUNK = 512
CHUNKS = 2


def shifted(shard, axis, by):
    peers = lax.axis_size(axis)
    pairs = [(i, i + by) for i in range(peers) if 0 <= i + by < peers]
    return lax.ppermute(shard, axis, pairs)


def lag_table(bins_count, lags_count, windows_all):
    bin_index = jnp.arange(bins_count, dtype=jnp.int32)
    lag_index = jnp.arange(lags_count, dtype=jnp.int32) - lags_count // 2
    phase_index = jnp.mod(bin_index[:, None] * lag_index[None, :], 2 * bins_count)
    angles = phase_index.astype(jnp.float32) * (jnp.pi / bins_count)
    window_taper = 0.5 + 0.5 * jnp.cos(lag_index.astype(jnp.float32) * (2.0 * jnp.pi / lags_count))
    norm_scale = 1.0 / jnp.sqrt(jnp.float32(2 * windows_all * bins_count))
    weights = (
        jnp.concatenate([jnp.cos(angles), -jnp.sin(angles)], 0)
        * (window_taper * norm_scale)[None, :]
    )
    return weights.astype(jnp.bfloat16)


def stack_kernel(n_win, n_comp, owners, lr_ref, li_ref, rr_ref, ri_ref, nr_ref, ni_ref, valid_ref, wr_ref, wi_ref, *rest):
    if len(rest) == 2:
        init_ref, out_ref = rest
    else:
        (out_ref,) = rest
        init_ref = None

    @pl.when(pl.program_id(0) == 0)
    def _():
        if init_ref is None:
            out_ref[...] = jnp.zeros_like(out_ref)
        else:
            out_ref[...] = init_ref[...]

    valid = valid_ref[...]
    wr = wr_ref[...]
    wi = wi_ref[...]
    slots = lr_ref.shape[1]
    for a in range(n_comp):
        lr = [lr_ref[w * n_comp + a].astype(jnp.float32) for w in range(n_win)]
        li = [li_ref[w * n_comp + a].astype(jnp.float32) for w in range(n_win)]
        for c in range(n_comp):
            re = None
            im = None
            for w in range(n_win):
                rr = rr_ref[w * n_comp + c].astype(jnp.float32) + nr_ref[w * n_comp + c].astype(jnp.float32)
                ri = ri_ref[w * n_comp + c].astype(jnp.float32) + ni_ref[w * n_comp + c].astype(jnp.float32)
                re_w = lr[w] * rr + li[w] * ri
                im_w = li[w] * rr - lr[w] * ri
                re = re_w if re is None else re + re_w
                im = im_w if im is None else im + im_w
            re = (re * valid).astype(jnp.bfloat16)
            im = (im * valid).astype(jnp.bfloat16)
            term = jnp.dot(re, wr, preferred_element_type=jnp.float32)
            term = term + jnp.dot(im, wi, preferred_element_type=jnp.float32)
            out_ref[a * n_comp + c] += term.reshape(owners, slots // owners, term.shape[-1])


def stacks_of(left, right, right_next, valid, lag_weights, owners, chunk, chunks, init=None):
    rows, slots, twice = left.shape
    bins_count = twice // 2
    n_comp = 3
    n_win = rows // n_comp
    steps = bins_count // CHUNK
    part = steps // chunks
    base = chunk * part
    lags = lag_weights.shape[1]
    left_re = pl.BlockSpec((rows, slots, CHUNK), lambda k: (0, 0, base + k))
    left_im = pl.BlockSpec((rows, slots, CHUNK), lambda k: (0, 0, base + k + steps))
    right_re = pl.BlockSpec((rows, slots, CHUNK), lambda k: (0, 0, k))
    right_im = pl.BlockSpec((rows, slots, CHUNK), lambda k: (0, 0, k + part))
    kernel = lambda *refs: stack_kernel(n_win, n_comp, owners, *refs)
    out_block = pl.BlockSpec((9, owners, slots // owners, lags), lambda k: (0, 0, 0, 0))
    extra = [] if init is None else [init]
    extra_specs = [] if init is None else [out_block]
    aliases = {} if init is None else {9: 0}
    flops = (2 * slots * 9 * twice * lags + 8 * slots * 9 * bins_count * n_win) // chunks
    bytes_accessed = (3 * left.size * 2 + lag_weights.size * 2) // chunks + owners * 9 * slots * lags * 4
    return pl.pallas_call(
        kernel,
        grid=(part,),
        in_specs=[
            left_re,
            left_im,
            left_re,
            left_im,
            right_re,
            right_im,
            pl.BlockSpec((slots, 1), lambda k: (0, 0)),
            pl.BlockSpec((CHUNK, lags), lambda k: (base + k, 0)),
            pl.BlockSpec((CHUNK, lags), lambda k: (base + k + steps, 0)),
        ]
        + extra_specs,
        out_specs=pl.BlockSpec((9, owners, slots // owners, lags), lambda k: (0, 0, 0, 0)),
        out_shape=jax.ShapeDtypeStruct((9, owners, slots // owners, lags), jnp.float32),
        compiler_params=pltpu.CompilerParams(
            dimension_semantics=("arbitrary",), vmem_limit_bytes=48 * 1024 * 1024
        ),
        cost_estimate=pl.CostEstimate(
            flops=flops, transcendentals=0, bytes_accessed=bytes_accessed
        ),
        input_output_aliases=aliases,
    )(left, left, right, right, right_next, right_next, valid, lag_weights, lag_weights, *extra)


def per_device(spectra, pair_first, pair_second, pair_count):
    n_w, block_size, n_c, twice = spectra.shape
    bins_count = twice // 2
    owners = lax.axis_size("win")
    block_index = lax.axis_index("pair")
    windows_all = n_w * owners
    chunks = CHUNKS
    width = bins_count // chunks
    halves = spectra[:, : block_size // 2].reshape(n_w, block_size // 2, n_c, 2, chunks, width)
    sent = [shifted(halves[:, :, :, :, q], "pair", -1) for q in range(chunks)]
    lag_weights = lag_table(bins_count, LAGS, windows_all)
    block_start = block_index * block_size
    first_local = pair_first[0] - block_start
    second_local = pair_second[0] - block_start
    slots = first_local.shape[0]
    slot_index = jnp.arange(slots, dtype=jnp.int32)
    valid = (slot_index < pair_count[0]).astype(jnp.float32)[:, None]

    own_rows = jnp.transpose(spectra, (0, 2, 1, 3)).reshape(n_w * n_c, block_size, twice)
    own_cols = jnp.arange(block_size, dtype=jnp.int32)
    next_cols = jnp.arange(block_size // 2, dtype=jnp.int32) + block_size
    pick_first = (first_local[:, None] == own_cols[None, :]).astype(jnp.bfloat16)
    pick_own = (second_local[:, None] == own_cols[None, :]).astype(jnp.bfloat16)
    pick_next = (second_local[:, None] == next_cols[None, :]).astype(jnp.bfloat16)
    left = jnp.einsum("ps,xsk->xpk", pick_first, own_rows, preferred_element_type=jnp.bfloat16)
    right = jnp.einsum("ps,xsk->xpk", pick_own, own_rows, preferred_element_type=jnp.bfloat16)

    partial = None
    for q in range(chunks):
        next_rows = jnp.transpose(sent[q], (0, 2, 1, 3, 4)).reshape(
            n_w * n_c, block_size // 2, 2 * width
        )
        picks = pick_next
        if partial is not None:
            picks, partial = lax.optimization_barrier((pick_next, partial))
        right_next = jnp.einsum("ps,xsk->xpk", picks, next_rows, preferred_element_type=jnp.bfloat16)
        partial = stacks_of(left, right, right_next, valid, lag_weights, owners, q, chunks, partial)
    partial = jnp.transpose(partial, (1, 0, 2, 3))
    received = lax.all_to_all(partial, "win", 0, 0, tiled=True)
    mine = jnp.sum(received, axis=0)
    return jnp.transpose(mine, (1, 0, 2))


def solution(mesh):
    return jax.shard_map(
        per_device,
        mesh=mesh,
        in_specs=(P("win", "pair", None, None), P("pair", None), P("pair", None), P("pair")),
        out_specs=P(("pair", "win"), None, None),
        check_vma=False,
    )
```

```python
import jax
import jax.numpy as jnp
from jax import lax
from jax.experimental import pallas as pl
from jax.experimental.pallas import tpu as pltpu
from jax.sharding import PartitionSpec as P

LAGS = 256
CHUNK = 512
CHUNKS = 4


def shifted(shard, axis, by):
    peers = lax.axis_size(axis)
    pairs = [(i, i + by) for i in range(peers) if 0 <= i + by < peers]
    return lax.ppermute(shard, axis, pairs)


def lag_table(bins_count, lags_count, windows_all):
    bin_index = jnp.arange(bins_count, dtype=jnp.int32)
    lag_index = jnp.arange(lags_count, dtype=jnp.int32) - lags_count // 2
    phase_index = jnp.mod(bin_index[:, None] * lag_index[None, :], 2 * bins_count)
    angles = phase_index.astype(jnp.float32) * (jnp.pi / bins_count)
    window_taper = 0.5 + 0.5 * jnp.cos(lag_index.astype(jnp.float32) * (2.0 * jnp.pi / lags_count))
    norm_scale = 1.0 / jnp.sqrt(jnp.float32(2 * windows_all * bins_count))
    weights = (
        jnp.concatenate([jnp.cos(angles), -jnp.sin(angles)], 0)
        * (window_taper * norm_scale)[None, :]
    )
    return weights.astype(jnp.bfloat16)


def stack_kernel(n_win, n_comp, owners, lr_ref, li_ref, rr_ref, ri_ref, nr_ref, ni_ref, valid_ref, wr_ref, wi_ref, *rest):
    if len(rest) == 2:
        init_ref, out_ref = rest
    else:
        (out_ref,) = rest
        init_ref = None

    @pl.when(pl.program_id(0) == 0)
    def _():
        if init_ref is None:
            out_ref[...] = jnp.zeros_like(out_ref)
        else:
            out_ref[...] = init_ref[...]

    valid = valid_ref[...]
    wr = wr_ref[...]
    wi = wi_ref[...]
    slots = lr_ref.shape[1]
    for a in range(n_comp):
        lr = [lr_ref[w * n_comp + a].astype(jnp.float32) for w in range(n_win)]
        li = [li_ref[w * n_comp + a].astype(jnp.float32) for w in range(n_win)]
        for c in range(n_comp):
            re = None
            im = None
            for w in range(n_win):
                rr = rr_ref[w * n_comp + c].astype(jnp.float32) + nr_ref[w * n_comp + c].astype(jnp.float32)
                ri = ri_ref[w * n_comp + c].astype(jnp.float32) + ni_ref[w * n_comp + c].astype(jnp.float32)
                re_w = lr[w] * rr + li[w] * ri
                im_w = li[w] * rr - lr[w] * ri
                re = re_w if re is None else re + re_w
                im = im_w if im is None else im + im_w
            re = (re * valid).astype(jnp.bfloat16)
            im = (im * valid).astype(jnp.bfloat16)
            term = jnp.dot(re, wr, preferred_element_type=jnp.float32)
            term = term + jnp.dot(im, wi, preferred_element_type=jnp.float32)
            out_ref[a * n_comp + c] += term.reshape(owners, slots // owners, term.shape[-1])


def stacks_of(left, right, right_next, valid, lag_weights, owners, chunk, chunks, init=None):
    rows, slots, twice = left.shape
    bins_count = twice // 2
    n_comp = 3
    n_win = rows // n_comp
    steps = bins_count // CHUNK
    part = steps // chunks
    base = chunk * part
    lags = lag_weights.shape[1]
    left_re = pl.BlockSpec((rows, slots, CHUNK), lambda k: (0, 0, base + k))
    left_im = pl.BlockSpec((rows, slots, CHUNK), lambda k: (0, 0, base + k + steps))
    right_re = pl.BlockSpec((rows, slots, CHUNK), lambda k: (0, 0, k))
    right_im = pl.BlockSpec((rows, slots, CHUNK), lambda k: (0, 0, k + part))
    kernel = lambda *refs: stack_kernel(n_win, n_comp, owners, *refs)
    out_block = pl.BlockSpec((9, owners, slots // owners, lags), lambda k: (0, 0, 0, 0))
    extra = [] if init is None else [init]
    extra_specs = [] if init is None else [out_block]
    aliases = {} if init is None else {9: 0}
    flops = (2 * slots * 9 * twice * lags + 8 * slots * 9 * bins_count * n_win) // chunks
    bytes_accessed = (3 * left.size * 2 + lag_weights.size * 2) // chunks + owners * 9 * slots * lags * 4
    return pl.pallas_call(
        kernel,
        grid=(part,),
        in_specs=[
            left_re,
            left_im,
            left_re,
            left_im,
            right_re,
            right_im,
            pl.BlockSpec((slots, 1), lambda k: (0, 0)),
            pl.BlockSpec((CHUNK, lags), lambda k: (base + k, 0)),
            pl.BlockSpec((CHUNK, lags), lambda k: (base + k + steps, 0)),
        ]
        + extra_specs,
        out_specs=pl.BlockSpec((9, owners, slots // owners, lags), lambda k: (0, 0, 0, 0)),
        out_shape=jax.ShapeDtypeStruct((9, owners, slots // owners, lags), jnp.float32),
        compiler_params=pltpu.CompilerParams(
            dimension_semantics=("arbitrary",), vmem_limit_bytes=48 * 1024 * 1024
        ),
        cost_estimate=pl.CostEstimate(
            flops=flops, transcendentals=0, bytes_accessed=bytes_accessed
        ),
        input_output_aliases=aliases,
    )(left, left, right, right, right_next, right_next, valid, lag_weights, lag_weights, *extra)


def per_device(spectra, pair_first, pair_second, pair_count):
    n_w, block_size, n_c, twice = spectra.shape
    bins_count = twice // 2
    owners = lax.axis_size("win")
    block_index = lax.axis_index("pair")
    windows_all = n_w * owners
    chunks = CHUNKS
    width = bins_count // chunks
    halves = spectra[:, : block_size // 2].reshape(n_w, block_size // 2, n_c, 2, chunks, width)
    sent = [shifted(halves[:, :, :, :, q], "pair", -1) for q in range(chunks)]
    lag_weights = lag_table(bins_count, LAGS, windows_all)
    block_start = block_index * block_size
    first_local = pair_first[0] - block_start
    second_local = pair_second[0] - block_start
    slots = first_local.shape[0]
    slot_index = jnp.arange(slots, dtype=jnp.int32)
    valid = (slot_index < pair_count[0]).astype(jnp.float32)[:, None]

    own_rows = jnp.transpose(spectra, (0, 2, 1, 3)).reshape(n_w * n_c, block_size, twice)
    own_cols = jnp.arange(block_size, dtype=jnp.int32)
    next_cols = jnp.arange(block_size // 2, dtype=jnp.int32) + block_size
    pick_first = (first_local[:, None] == own_cols[None, :]).astype(jnp.bfloat16)
    pick_own = (second_local[:, None] == own_cols[None, :]).astype(jnp.bfloat16)
    pick_next = (second_local[:, None] == next_cols[None, :]).astype(jnp.bfloat16)
    left = jnp.einsum("ps,xsk->xpk", pick_first, own_rows, preferred_element_type=jnp.bfloat16)
    right = jnp.einsum("ps,xsk->xpk", pick_own, own_rows, preferred_element_type=jnp.bfloat16)

    partial = None
    for q in range(chunks):
        next_rows = jnp.transpose(sent[q], (0, 2, 1, 3, 4)).reshape(
            n_w * n_c, block_size // 2, 2 * width
        )
        picks = pick_next
        if partial is not None:
            picks, partial = lax.optimization_barrier((pick_next, partial))
        right_next = jnp.einsum("ps,xsk->xpk", picks, next_rows, preferred_element_type=jnp.bfloat16)
        partial = stacks_of(left, right, right_next, valid, lag_weights, owners, q, chunks, partial)
    partial = jnp.transpose(partial, (1, 0, 2, 3))
    received = lax.all_to_all(partial, "win", 0, 0, tiled=True)
    mine = jnp.sum(received, axis=0)
    return jnp.transpose(mine, (1, 0, 2))


def solution(mesh):
    return jax.shard_map(
        per_device,
        mesh=mesh,
        in_specs=(P("win", "pair", None, None), P("pair", None), P("pair", None), P("pair")),
        out_specs=P(("pair", "win"), None, None),
        check_vma=False,
    )
```

```python
import jax
import jax.numpy as jnp
from jax import lax
from jax.experimental import pallas as pl
from jax.experimental.pallas import tpu as pltpu
from jax.sharding import PartitionSpec as P

LAGS = 256
CHUNK = 512
CHUNKS = 4


def shifted(shard, axis, by):
    peers = lax.axis_size(axis)
    pairs = [(i, i + by) for i in range(peers) if 0 <= i + by < peers]
    return lax.ppermute(shard, axis, pairs)


def lag_table(bins_count, lags_count, windows_all):
    lag_index = jnp.arange(lags_count, dtype=jnp.int32) - lags_count // 2
    window_taper = 0.5 + 0.5 * jnp.cos(lag_index.astype(jnp.float32) * (2.0 * jnp.pi / lags_count))
    norm_scale = 1.0 / jnp.sqrt(jnp.float32(2 * windows_all * bins_count))
    scale = (window_taper * norm_scale)[None, None, :]
    fine_count = 64
    coarse_count = bins_count // fine_count
    coarse = jnp.arange(coarse_count, dtype=jnp.int32) * fine_count
    fine = jnp.arange(fine_count, dtype=jnp.int32)

    def phase(bins):
        turns = jnp.mod(bins[:, None] * lag_index[None, :], 2 * bins_count)
        angles = turns.astype(jnp.float32) * (jnp.pi / bins_count)
        return jnp.cos(angles), jnp.sin(angles)

    cos_a, sin_a = phase(coarse)
    cos_b, sin_b = phase(fine)
    cos_a, sin_a = cos_a[:, None, :], sin_a[:, None, :]
    cos_b, sin_b = cos_b[None, :, :], sin_b[None, :, :]
    cos_ab = (cos_a * cos_b - sin_a * sin_b) * scale
    sin_ab = (sin_a * cos_b + cos_a * sin_b) * scale
    weights = jnp.concatenate(
        [cos_ab.reshape(bins_count, lags_count), -sin_ab.reshape(bins_count, lags_count)], 0
    )
    return weights.astype(jnp.bfloat16)


def stack_kernel(n_win, n_comp, owners, lr_ref, li_ref, rr_ref, ri_ref, nr_ref, ni_ref, valid_ref, wr_ref, wi_ref, *rest):
    if len(rest) == 2:
        init_ref, out_ref = rest
    else:
        (out_ref,) = rest
        init_ref = None

    @pl.when(pl.program_id(0) == 0)
    def _():
        if init_ref is None:
            out_ref[...] = jnp.zeros_like(out_ref)
        else:
            out_ref[...] = init_ref[...]

    valid = valid_ref[...]
    wr = wr_ref[...]
    wi = wi_ref[...]
    slots = lr_ref.shape[1]
    for a in range(n_comp):
        lr = [lr_ref[w * n_comp + a].astype(jnp.float32) for w in range(n_win)]
        li = [li_ref[w * n_comp + a].astype(jnp.float32) for w in range(n_win)]
        for c in range(n_comp):
            re = None
            im = None
            for w in range(n_win):
                rr = rr_ref[w * n_comp + c].astype(jnp.float32) + nr_ref[w * n_comp + c].astype(jnp.float32)
                ri = ri_ref[w * n_comp + c].astype(jnp.float32) + ni_ref[w * n_comp + c].astype(jnp.float32)
                re_w = lr[w] * rr + li[w] * ri
                im_w = li[w] * rr - lr[w] * ri
                re = re_w if re is None else re + re_w
                im = im_w if im is None else im + im_w
            re = (re * valid).astype(jnp.bfloat16)
            im = (im * valid).astype(jnp.bfloat16)
            term = jnp.dot(re, wr, preferred_element_type=jnp.float32)
            term = term + jnp.dot(im, wi, preferred_element_type=jnp.float32)
            out_ref[a * n_comp + c] += term.reshape(owners, slots // owners, term.shape[-1])


def stacks_of(left, right, right_next, valid, lag_weights, owners, chunk, chunks, init=None):
    rows, slots, twice = left.shape
    bins_count = twice // 2
    n_comp = 3
    n_win = rows // n_comp
    steps = bins_count // CHUNK
    part = steps // chunks
    base = chunk * part
    lags = lag_weights.shape[1]
    left_re = pl.BlockSpec((rows, slots, CHUNK), lambda k: (0, 0, base + k))
    left_im = pl.BlockSpec((rows, slots, CHUNK), lambda k: (0, 0, base + k + steps))
    right_re = pl.BlockSpec((rows, slots, CHUNK), lambda k: (0, 0, k))
    right_im = pl.BlockSpec((rows, slots, CHUNK), lambda k: (0, 0, k + part))
    kernel = lambda *refs: stack_kernel(n_win, n_comp, owners, *refs)
    out_block = pl.BlockSpec((9, owners, slots // owners, lags), lambda k: (0, 0, 0, 0))
    extra = [] if init is None else [init]
    extra_specs = [] if init is None else [out_block]
    aliases = {} if init is None else {9: 0}
    flops = (2 * slots * 9 * twice * lags + 8 * slots * 9 * bins_count * n_win) // chunks
    bytes_accessed = (3 * left.size * 2 + lag_weights.size * 2) // chunks + owners * 9 * slots * lags * 4
    return pl.pallas_call(
        kernel,
        grid=(part,),
        in_specs=[
            left_re,
            left_im,
            left_re,
            left_im,
            right_re,
            right_im,
            pl.BlockSpec((slots, 1), lambda k: (0, 0)),
            pl.BlockSpec((CHUNK, lags), lambda k: (base + k, 0)),
            pl.BlockSpec((CHUNK, lags), lambda k: (base + k + steps, 0)),
        ]
        + extra_specs,
        out_specs=pl.BlockSpec((9, owners, slots // owners, lags), lambda k: (0, 0, 0, 0)),
        out_shape=jax.ShapeDtypeStruct((9, owners, slots // owners, lags), jnp.float32),
        compiler_params=pltpu.CompilerParams(
            dimension_semantics=("arbitrary",), vmem_limit_bytes=48 * 1024 * 1024
        ),
        cost_estimate=pl.CostEstimate(
            flops=flops, transcendentals=0, bytes_accessed=bytes_accessed
        ),
        input_output_aliases=aliases,
    )(left, left, right, right, right_next, right_next, valid, lag_weights, lag_weights, *extra)


def per_device(spectra, pair_first, pair_second, pair_count):
    n_w, block_size, n_c, twice = spectra.shape
    bins_count = twice // 2
    owners = lax.axis_size("win")
    block_index = lax.axis_index("pair")
    windows_all = n_w * owners
    chunks = CHUNKS
    width = bins_count // chunks
    halves = spectra[:, : block_size // 2].reshape(n_w, block_size // 2, n_c, 2, chunks, width)
    peers = lax.axis_size("pair")
    cut = peers // 2
    relay = 1 if peers >= 4 else None
    sent = []
    for q in range(chunks):
        piece = halves[:, :, :, :, q]
        if relay is None or q < chunks // 2:
            sent.append(shifted(piece, "pair", -1))
            continue
        direct = lax.ppermute(piece, "pair", [(i, i - 1) for i in range(1, peers) if i != cut])
        hop = lax.ppermute(piece, "pair", [(cut, relay)])
        sent.append(direct + lax.ppermute(hop, "pair", [(relay, cut - 1)]))
    lag_weights = lag_table(bins_count, LAGS, windows_all)
    block_start = block_index * block_size
    first_local = pair_first[0] - block_start
    second_local = pair_second[0] - block_start
    slots = first_local.shape[0]
    slot_index = jnp.arange(slots, dtype=jnp.int32)
    valid = (slot_index < pair_count[0]).astype(jnp.float32)[:, None]

    own_rows = jnp.transpose(spectra, (0, 2, 1, 3)).reshape(n_w * n_c, block_size, twice)
    own_cols = jnp.arange(block_size, dtype=jnp.int32)
    next_cols = jnp.arange(block_size // 2, dtype=jnp.int32) + block_size
    pick_first = (first_local[:, None] == own_cols[None, :]).astype(jnp.bfloat16)
    pick_own = (second_local[:, None] == own_cols[None, :]).astype(jnp.bfloat16)
    pick_next = (second_local[:, None] == next_cols[None, :]).astype(jnp.bfloat16)
    left = jnp.einsum("ps,xsk->xpk", pick_first, own_rows, preferred_element_type=jnp.bfloat16)
    right = jnp.einsum("ps,xsk->xpk", pick_own, own_rows, preferred_element_type=jnp.bfloat16)

    partial = None
    for q in range(chunks):
        next_rows = jnp.transpose(sent[q], (0, 2, 1, 3, 4)).reshape(
            n_w * n_c, block_size // 2, 2 * width
        )
        picks = pick_next
        if partial is not None:
            picks, partial = lax.optimization_barrier((pick_next, partial))
        right_next = jnp.einsum("ps,xsk->xpk", picks, next_rows, preferred_element_type=jnp.bfloat16)
        partial = stacks_of(left, right, right_next, valid, lag_weights, owners, q, chunks, partial)
    partial = jnp.transpose(partial, (1, 0, 2, 3))
    received = lax.all_to_all(partial, "win", 0, 0, tiled=True)
    mine = jnp.sum(received, axis=0)
    return jnp.transpose(mine, (1, 0, 2))


def solution(mesh):
    return jax.shard_map(
        per_device,
        mesh=mesh,
        in_specs=(P("win", "pair", None, None), P("pair", None), P("pair", None), P("pair")),
        out_specs=P(("pair", "win"), None, None),
        check_vma=False,
    )
```

```python
import jax
import jax.numpy as jnp
from jax import lax
from jax.experimental import pallas as pl
from jax.experimental.pallas import tpu as pltpu
from jax.sharding import PartitionSpec as P

LAGS = 256
CHUNK = 512
CHUNKS = 2


def shifted(shard, axis, by):
    peers = lax.axis_size(axis)
    pairs = [(i, i + by) for i in range(peers) if 0 <= i + by < peers]
    return lax.ppermute(shard, axis, pairs)


def lag_table(bins_count, lags_count, windows_all):
    lag_index = jnp.arange(lags_count, dtype=jnp.int32) - lags_count // 2
    window_taper = 0.5 + 0.5 * jnp.cos(lag_index.astype(jnp.float32) * (2.0 * jnp.pi / lags_count))
    norm_scale = 1.0 / jnp.sqrt(jnp.float32(2 * windows_all * bins_count))
    scale = (window_taper * norm_scale)[None, None, :]
    fine_count = 64
    coarse_count = bins_count // fine_count
    coarse = jnp.arange(coarse_count, dtype=jnp.int32) * fine_count
    fine = jnp.arange(fine_count, dtype=jnp.int32)

    def phase(bins):
        turns = jnp.mod(bins[:, None] * lag_index[None, :], 2 * bins_count)
        angles = turns.astype(jnp.float32) * (jnp.pi / bins_count)
        return jnp.cos(angles), jnp.sin(angles)

    cos_a, sin_a = phase(coarse)
    cos_b, sin_b = phase(fine)
    cos_a, sin_a = cos_a[:, None, :], sin_a[:, None, :]
    cos_b, sin_b = cos_b[None, :, :], sin_b[None, :, :]
    cos_ab = (cos_a * cos_b - sin_a * sin_b) * scale
    sin_ab = (sin_a * cos_b + cos_a * sin_b) * scale
    weights = jnp.concatenate(
        [cos_ab.reshape(bins_count, lags_count), -sin_ab.reshape(bins_count, lags_count)], 0
    )
    return weights.astype(jnp.bfloat16)


def stack_kernel(n_win, n_comp, owners, lr_ref, li_ref, rr_ref, ri_ref, nr_ref, ni_ref, valid_ref, wr_ref, wi_ref, *rest):
    if len(rest) == 2:
        init_ref, out_ref = rest
    else:
        (out_ref,) = rest
        init_ref = None

    @pl.when(pl.program_id(0) == 0)
    def _():
        if init_ref is None:
            out_ref[...] = jnp.zeros_like(out_ref)
        else:
            out_ref[...] = init_ref[...]

    valid = valid_ref[...]
    wr = wr_ref[...]
    wi = wi_ref[...]
    slots = lr_ref.shape[1]
    for a in range(n_comp):
        lr = [lr_ref[w * n_comp + a].astype(jnp.float32) for w in range(n_win)]
        li = [li_ref[w * n_comp + a].astype(jnp.float32) for w in range(n_win)]
        for c in range(n_comp):
            re = None
            im = None
            for w in range(n_win):
                rr = rr_ref[w * n_comp + c].astype(jnp.float32) + nr_ref[w * n_comp + c].astype(jnp.float32)
                ri = ri_ref[w * n_comp + c].astype(jnp.float32) + ni_ref[w * n_comp + c].astype(jnp.float32)
                re_w = lr[w] * rr + li[w] * ri
                im_w = li[w] * rr - lr[w] * ri
                re = re_w if re is None else re + re_w
                im = im_w if im is None else im + im_w
            re = (re * valid).astype(jnp.bfloat16)
            im = (im * valid).astype(jnp.bfloat16)
            term = jnp.dot(re, wr, preferred_element_type=jnp.float32)
            term = term + jnp.dot(im, wi, preferred_element_type=jnp.float32)
            out_ref[a * n_comp + c] += term.reshape(owners, slots // owners, term.shape[-1])


def stacks_of(left, right, right_next, valid, lag_weights, owners, chunk, chunks, init=None):
    rows, slots, twice = left.shape
    bins_count = twice // 2
    n_comp = 3
    n_win = rows // n_comp
    steps = bins_count // CHUNK
    part = steps // chunks
    base = chunk * part
    lags = lag_weights.shape[1]
    left_re = pl.BlockSpec((rows, slots, CHUNK), lambda k: (0, 0, base + k))
    left_im = pl.BlockSpec((rows, slots, CHUNK), lambda k: (0, 0, base + k + steps))
    right_re = pl.BlockSpec((rows, slots, CHUNK), lambda k: (0, 0, k))
    right_im = pl.BlockSpec((rows, slots, CHUNK), lambda k: (0, 0, k + part))
    kernel = lambda *refs: stack_kernel(n_win, n_comp, owners, *refs)
    out_block = pl.BlockSpec((9, owners, slots // owners, lags), lambda k: (0, 0, 0, 0))
    extra = [] if init is None else [init]
    extra_specs = [] if init is None else [out_block]
    aliases = {} if init is None else {9: 0}
    flops = (2 * slots * 9 * twice * lags + 8 * slots * 9 * bins_count * n_win) // chunks
    bytes_accessed = (3 * left.size * 2 + lag_weights.size * 2) // chunks + owners * 9 * slots * lags * 4
    return pl.pallas_call(
        kernel,
        grid=(part,),
        in_specs=[
            left_re,
            left_im,
            left_re,
            left_im,
            right_re,
            right_im,
            pl.BlockSpec((slots, 1), lambda k: (0, 0)),
            pl.BlockSpec((CHUNK, lags), lambda k: (base + k, 0)),
            pl.BlockSpec((CHUNK, lags), lambda k: (base + k + steps, 0)),
        ]
        + extra_specs,
        out_specs=pl.BlockSpec((9, owners, slots // owners, lags), lambda k: (0, 0, 0, 0)),
        out_shape=jax.ShapeDtypeStruct((9, owners, slots // owners, lags), jnp.float32),
        compiler_params=pltpu.CompilerParams(
            dimension_semantics=("arbitrary",), vmem_limit_bytes=48 * 1024 * 1024
        ),
        cost_estimate=pl.CostEstimate(
            flops=flops, transcendentals=0, bytes_accessed=bytes_accessed
        ),
        input_output_aliases=aliases,
    )(left, left, right, right, right_next, right_next, valid, lag_weights, lag_weights, *extra)


def per_device(spectra, pair_first, pair_second, pair_count):
    n_w, block_size, n_c, twice = spectra.shape
    bins_count = twice // 2
    owners = lax.axis_size("win")
    block_index = lax.axis_index("pair")
    windows_all = n_w * owners
    chunks = CHUNKS
    width = bins_count // chunks
    halves = spectra[:, : block_size // 2].reshape(n_w, block_size // 2, n_c, 2, chunks, width)
    peers = lax.axis_size("pair")
    cut = peers // 2
    relay = 1 if peers >= 4 else None
    sent = []
    for q in range(chunks):
        piece = halves[:, :, :, :, q]
        if relay is None or q < chunks // 2:
            sent.append(shifted(piece, "pair", -1))
            continue
        direct = lax.ppermute(piece, "pair", [(i, i - 1) for i in range(1, peers) if i != cut])
        hop = lax.ppermute(piece, "pair", [(cut, relay)])
        sent.append(direct + lax.ppermute(hop, "pair", [(relay, cut - 1)]))
    lag_weights = lag_table(bins_count, LAGS, windows_all)
    block_start = block_index * block_size
    first_local = pair_first[0] - block_start
    second_local = pair_second[0] - block_start
    slots = first_local.shape[0]
    slot_index = jnp.arange(slots, dtype=jnp.int32)
    valid = (slot_index < pair_count[0]).astype(jnp.float32)[:, None]

    own_rows = jnp.transpose(spectra, (0, 2, 1, 3)).reshape(n_w * n_c, block_size, twice)
    own_cols = jnp.arange(block_size, dtype=jnp.int32)
    next_cols = jnp.arange(block_size // 2, dtype=jnp.int32) + block_size
    pick_first = (first_local[:, None] == own_cols[None, :]).astype(jnp.bfloat16)
    pick_own = (second_local[:, None] == own_cols[None, :]).astype(jnp.bfloat16)
    pick_next = (second_local[:, None] == next_cols[None, :]).astype(jnp.bfloat16)
    left = jnp.einsum("ps,xsk->xpk", pick_first, own_rows, preferred_element_type=jnp.bfloat16)
    right = jnp.einsum("ps,xsk->xpk", pick_own, own_rows, preferred_element_type=jnp.bfloat16)

    partial = None
    for q in range(chunks):
        next_rows = jnp.transpose(sent[q], (0, 2, 1, 3, 4)).reshape(
            n_w * n_c, block_size // 2, 2 * width
        )
        picks = pick_next
        if partial is not None:
            picks, partial = lax.optimization_barrier((pick_next, partial))
        right_next = jnp.einsum("ps,xsk->xpk", picks, next_rows, preferred_element_type=jnp.bfloat16)
        partial = stacks_of(left, right, right_next, valid, lag_weights, owners, q, chunks, partial)
    partial = jnp.transpose(partial, (1, 0, 2, 3))
    received = lax.all_to_all(partial, "win", 0, 0, tiled=True)
    mine = jnp.sum(received, axis=0)
    return jnp.transpose(mine, (1, 0, 2))


def solution(mesh):
    return jax.shard_map(
        per_device,
        mesh=mesh,
        in_specs=(P("win", "pair", None, None), P("pair", None), P("pair", None), P("pair")),
        out_specs=P(("pair", "win"), None, None),
        check_vma=False,
    )
```

```python
import jax
import jax.numpy as jnp
from jax import lax
from jax.experimental import pallas as pl
from jax.experimental.pallas import tpu as pltpu
from jax.sharding import PartitionSpec as P

LAGS = 256
CHUNK = 512
CHUNKS = 4


def shifted(shard, axis, by):
    peers = lax.axis_size(axis)
    pairs = [(i, i + by) for i in range(peers) if 0 <= i + by < peers]
    return lax.ppermute(shard, axis, pairs)


def lag_table(bins_count, lags_count, windows_all):
    lag_index = jnp.arange(lags_count, dtype=jnp.int32) - lags_count // 2
    window_taper = 0.5 + 0.5 * jnp.cos(lag_index.astype(jnp.float32) * (2.0 * jnp.pi / lags_count))
    norm_scale = 1.0 / jnp.sqrt(jnp.float32(2 * windows_all * bins_count))
    scale = (window_taper * norm_scale)[None, None, :]
    fine_count = 64
    coarse_count = bins_count // fine_count
    coarse = jnp.arange(coarse_count, dtype=jnp.int32) * fine_count
    fine = jnp.arange(fine_count, dtype=jnp.int32)

    def phase(bins):
        turns = jnp.mod(bins[:, None] * lag_index[None, :], 2 * bins_count)
        angles = turns.astype(jnp.float32) * (jnp.pi / bins_count)
        return jnp.cos(angles), jnp.sin(angles)

    cos_a, sin_a = phase(coarse)
    cos_b, sin_b = phase(fine)
    cos_a, sin_a = cos_a[:, None, :], sin_a[:, None, :]
    cos_b, sin_b = cos_b[None, :, :], sin_b[None, :, :]
    cos_ab = (cos_a * cos_b - sin_a * sin_b) * scale
    sin_ab = (sin_a * cos_b + cos_a * sin_b) * scale
    weights = jnp.concatenate(
        [cos_ab.reshape(bins_count, lags_count), -sin_ab.reshape(bins_count, lags_count)], 0
    )
    return weights.astype(jnp.bfloat16)


def stack_kernel(n_win, n_comp, owners, lr_ref, li_ref, rr_ref, ri_ref, nr_ref, ni_ref, valid_ref, wr_ref, wi_ref, *rest):
    if len(rest) == 2:
        init_ref, out_ref = rest
    else:
        (out_ref,) = rest
        init_ref = None

    @pl.when(pl.program_id(0) == 0)
    def _():
        if init_ref is None:
            out_ref[...] = jnp.zeros_like(out_ref)
        else:
            out_ref[...] = init_ref[...]

    valid = valid_ref[...]
    wr = wr_ref[...]
    wi = wi_ref[...]
    slots = lr_ref.shape[1]
    for a in range(n_comp):
        lr = [lr_ref[w * n_comp + a].astype(jnp.float32) for w in range(n_win)]
        li = [li_ref[w * n_comp + a].astype(jnp.float32) for w in range(n_win)]
        for c in range(n_comp):
            re = None
            im = None
            for w in range(n_win):
                rr = rr_ref[w * n_comp + c].astype(jnp.float32) + nr_ref[w * n_comp + c].astype(jnp.float32)
                ri = ri_ref[w * n_comp + c].astype(jnp.float32) + ni_ref[w * n_comp + c].astype(jnp.float32)
                re_w = lr[w] * rr + li[w] * ri
                im_w = li[w] * rr - lr[w] * ri
                re = re_w if re is None else re + re_w
                im = im_w if im is None else im + im_w
            re = (re * valid).astype(jnp.bfloat16)
            im = (im * valid).astype(jnp.bfloat16)
            term = jnp.dot(re, wr, preferred_element_type=jnp.float32)
            term = term + jnp.dot(im, wi, preferred_element_type=jnp.float32)
            out_ref[a * n_comp + c] += term.reshape(owners, slots // owners, term.shape[-1])


def stacks_of(left, right, right_next, valid, lag_weights, owners, chunk, chunks, init=None):
    rows, both_slots, twice = left.shape
    slots = both_slots // 2
    bins_count = twice // 2
    n_comp = 3
    n_win = rows // n_comp
    steps = bins_count // CHUNK
    part = steps // chunks
    base = chunk * part
    lags = lag_weights.shape[1]
    left_re = pl.BlockSpec((rows, slots, CHUNK), lambda k: (0, 0, base + k))
    left_im = pl.BlockSpec((rows, slots, CHUNK), lambda k: (0, 0, base + k + steps))
    own_re = pl.BlockSpec((rows, slots, CHUNK), lambda k: (0, 1, base + k))
    own_im = pl.BlockSpec((rows, slots, CHUNK), lambda k: (0, 1, base + k + steps))
    right_re = pl.BlockSpec((rows, slots, CHUNK), lambda k: (0, 0, k))
    right_im = pl.BlockSpec((rows, slots, CHUNK), lambda k: (0, 0, k + part))
    kernel = lambda *refs: stack_kernel(n_win, n_comp, owners, *refs)
    out_block = pl.BlockSpec((9, owners, slots // owners, lags), lambda k: (0, 0, 0, 0))
    extra = [] if init is None else [init]
    extra_specs = [] if init is None else [out_block]
    aliases = {} if init is None else {9: 0}
    flops = (2 * slots * 9 * twice * lags + 8 * slots * 9 * bins_count * n_win) // chunks
    bytes_accessed = (3 * left.size + lag_weights.size * 2) // chunks + owners * 9 * slots * lags * 4
    return pl.pallas_call(
        kernel,
        grid=(part,),
        in_specs=[
            left_re,
            left_im,
            own_re,
            own_im,
            right_re,
            right_im,
            pl.BlockSpec((slots, 1), lambda k: (0, 0)),
            pl.BlockSpec((CHUNK, lags), lambda k: (base + k, 0)),
            pl.BlockSpec((CHUNK, lags), lambda k: (base + k + steps, 0)),
        ]
        + extra_specs,
        out_specs=pl.BlockSpec((9, owners, slots // owners, lags), lambda k: (0, 0, 0, 0)),
        out_shape=jax.ShapeDtypeStruct((9, owners, slots // owners, lags), jnp.float32),
        compiler_params=pltpu.CompilerParams(
            dimension_semantics=("arbitrary",), vmem_limit_bytes=48 * 1024 * 1024
        ),
        cost_estimate=pl.CostEstimate(
            flops=flops, transcendentals=0, bytes_accessed=bytes_accessed
        ),
        input_output_aliases=aliases,
    )(left, left, right, right, right_next, right_next, valid, lag_weights, lag_weights, *extra)


def per_device(spectra, pair_first, pair_second, pair_count):
    n_w, block_size, n_c, twice = spectra.shape
    bins_count = twice // 2
    owners = lax.axis_size("win")
    block_index = lax.axis_index("pair")
    windows_all = n_w * owners
    chunks = CHUNKS
    width = bins_count // chunks
    halves = spectra[:, : block_size // 2].reshape(n_w, block_size // 2, n_c, 2, chunks, width)
    peers = lax.axis_size("pair")
    cut = peers // 2
    relay = 1 if peers >= 4 else None
    sent = []
    for q in range(chunks):
        piece = halves[:, :, :, :, q]
        if relay is None or q < chunks // 2:
            sent.append(shifted(piece, "pair", -1))
            continue
        direct = lax.ppermute(piece, "pair", [(i, i - 1) for i in range(1, peers) if i != cut])
        hop = lax.ppermute(piece, "pair", [(cut, relay)])
        sent.append(direct + lax.ppermute(hop, "pair", [(relay, cut - 1)]))
    lag_weights = lag_table(bins_count, LAGS, windows_all)
    block_start = block_index * block_size
    first_local = pair_first[0] - block_start
    second_local = pair_second[0] - block_start
    slots = first_local.shape[0]
    slot_index = jnp.arange(slots, dtype=jnp.int32)
    valid = (slot_index < pair_count[0]).astype(jnp.float32)[:, None]

    own_rows = jnp.transpose(spectra, (0, 2, 1, 3)).reshape(n_w * n_c, block_size, twice)
    own_cols = jnp.arange(block_size, dtype=jnp.int32)
    next_cols = jnp.arange(block_size // 2, dtype=jnp.int32) + block_size
    pick_first = (first_local[:, None] == own_cols[None, :]).astype(jnp.bfloat16)
    pick_own = (second_local[:, None] == own_cols[None, :]).astype(jnp.bfloat16)
    pick_next = (second_local[:, None] == next_cols[None, :]).astype(jnp.bfloat16)
    picks_own = jnp.concatenate([pick_first, pick_own], axis=0)
    left = jnp.einsum("ps,xsk->xpk", picks_own, own_rows, preferred_element_type=jnp.bfloat16)
    right = left

    partial = None
    for q in range(chunks):
        next_rows = jnp.transpose(sent[q], (0, 2, 1, 3, 4)).reshape(
            n_w * n_c, block_size // 2, 2 * width
        )
        picks = pick_next
        if partial is not None:
            picks, partial = lax.optimization_barrier((pick_next, partial))
        right_next = jnp.einsum("ps,xsk->xpk", picks, next_rows, preferred_element_type=jnp.bfloat16)
        partial = stacks_of(left, right, right_next, valid, lag_weights, owners, q, chunks, partial)
    partial = jnp.transpose(partial, (1, 0, 2, 3))
    received = lax.all_to_all(partial, "win", 0, 0, tiled=True)
    mine = jnp.sum(received, axis=0)
    return jnp.transpose(mine, (1, 0, 2))


def solution(mesh):
    return jax.shard_map(
        per_device,
        mesh=mesh,
        in_specs=(P("win", "pair", None, None), P("pair", None), P("pair", None), P("pair")),
        out_specs=P(("pair", "win"), None, None),
        check_vma=False,
    )
```

```python
import jax
import jax.numpy as jnp
from jax import lax
from jax.experimental import pallas as pl
from jax.experimental.pallas import tpu as pltpu
from jax.sharding import PartitionSpec as P

LAGS = 256
CHUNK = 256
CHUNKS = 4


def shifted(shard, axis, by):
    peers = lax.axis_size(axis)
    pairs = [(i, i + by) for i in range(peers) if 0 <= i + by < peers]
    return lax.ppermute(shard, axis, pairs)


def lag_table(bins_count, lags_count, windows_all):
    lag_index = jnp.arange(lags_count, dtype=jnp.int32) - lags_count // 2
    window_taper = 0.5 + 0.5 * jnp.cos(lag_index.astype(jnp.float32) * (2.0 * jnp.pi / lags_count))
    norm_scale = 1.0 / jnp.sqrt(jnp.float32(2 * windows_all * bins_count))
    scale = (window_taper * norm_scale)[None, None, :]
    fine_count = 64
    coarse_count = bins_count // fine_count
    coarse = jnp.arange(coarse_count, dtype=jnp.int32) * fine_count
    fine = jnp.arange(fine_count, dtype=jnp.int32)

    def phase(bins):
        turns = jnp.mod(bins[:, None] * lag_index[None, :], 2 * bins_count)
        angles = turns.astype(jnp.float32) * (jnp.pi / bins_count)
        return jnp.cos(angles), jnp.sin(angles)

    cos_a, sin_a = phase(coarse)
    cos_b, sin_b = phase(fine)
    cos_a, sin_a = cos_a[:, None, :], sin_a[:, None, :]
    cos_b, sin_b = cos_b[None, :, :], sin_b[None, :, :]
    cos_ab = (cos_a * cos_b - sin_a * sin_b) * scale
    sin_ab = (sin_a * cos_b + cos_a * sin_b) * scale
    weights = jnp.concatenate(
        [cos_ab.reshape(bins_count, lags_count), -sin_ab.reshape(bins_count, lags_count)], 0
    )
    return weights.astype(jnp.bfloat16)


def stack_kernel(n_win, n_comp, owners, lr_ref, li_ref, rr_ref, ri_ref, nr_ref, ni_ref, valid_ref, wr_ref, wi_ref, *rest):
    if len(rest) == 2:
        init_ref, out_ref = rest
    else:
        (out_ref,) = rest
        init_ref = None

    @pl.when(pl.program_id(0) == 0)
    def _():
        if init_ref is None:
            out_ref[...] = jnp.zeros_like(out_ref)
        else:
            out_ref[...] = init_ref[...]

    valid = valid_ref[...]
    wr = wr_ref[...]
    wi = wi_ref[...]
    slots = lr_ref.shape[1]
    for a in range(n_comp):
        lr = [lr_ref[w * n_comp + a].astype(jnp.float32) for w in range(n_win)]
        li = [li_ref[w * n_comp + a].astype(jnp.float32) for w in range(n_win)]
        for c in range(n_comp):
            re = None
            im = None
            for w in range(n_win):
                rr = rr_ref[w * n_comp + c].astype(jnp.float32) + nr_ref[w * n_comp + c].astype(jnp.float32)
                ri = ri_ref[w * n_comp + c].astype(jnp.float32) + ni_ref[w * n_comp + c].astype(jnp.float32)
                re_w = lr[w] * rr + li[w] * ri
                im_w = li[w] * rr - lr[w] * ri
                re = re_w if re is None else re + re_w
                im = im_w if im is None else im + im_w
            re = (re * valid).astype(jnp.bfloat16)
            im = (im * valid).astype(jnp.bfloat16)
            term = jnp.dot(re, wr, preferred_element_type=jnp.float32)
            term = term + jnp.dot(im, wi, preferred_element_type=jnp.float32)
            out_ref[a * n_comp + c] += term.reshape(owners, slots // owners, term.shape[-1])


def stacks_of(left, right, right_next, valid, lag_weights, owners, chunk, chunks, init=None):
    rows, slots, twice = left.shape
    bins_count = twice // 2
    n_comp = 3
    n_win = rows // n_comp
    steps = bins_count // CHUNK
    part = steps // chunks
    base = chunk * part
    lags = lag_weights.shape[1]
    left_re = pl.BlockSpec((rows, slots, CHUNK), lambda k: (0, 0, base + k))
    left_im = pl.BlockSpec((rows, slots, CHUNK), lambda k: (0, 0, base + k + steps))
    right_re = pl.BlockSpec((rows, slots, CHUNK), lambda k: (0, 0, k))
    right_im = pl.BlockSpec((rows, slots, CHUNK), lambda k: (0, 0, k + part))
    kernel = lambda *refs: stack_kernel(n_win, n_comp, owners, *refs)
    out_block = pl.BlockSpec((9, owners, slots // owners, lags), lambda k: (0, 0, 0, 0))
    extra = [] if init is None else [init]
    extra_specs = [] if init is None else [out_block]
    aliases = {} if init is None else {9: 0}
    flops = (2 * slots * 9 * twice * lags + 8 * slots * 9 * bins_count * n_win) // chunks
    bytes_accessed = (3 * left.size * 2 + lag_weights.size * 2) // chunks + owners * 9 * slots * lags * 4
    return pl.pallas_call(
        kernel,
        grid=(part,),
        in_specs=[
            left_re,
            left_im,
            left_re,
            left_im,
            right_re,
            right_im,
            pl.BlockSpec((slots, 1), lambda k: (0, 0)),
            pl.BlockSpec((CHUNK, lags), lambda k: (base + k, 0)),
            pl.BlockSpec((CHUNK, lags), lambda k: (base + k + steps, 0)),
        ]
        + extra_specs,
        out_specs=pl.BlockSpec((9, owners, slots // owners, lags), lambda k: (0, 0, 0, 0)),
        out_shape=jax.ShapeDtypeStruct((9, owners, slots // owners, lags), jnp.float32),
        compiler_params=pltpu.CompilerParams(
            dimension_semantics=("arbitrary",), vmem_limit_bytes=48 * 1024 * 1024
        ),
        cost_estimate=pl.CostEstimate(
            flops=flops, transcendentals=0, bytes_accessed=bytes_accessed
        ),
        input_output_aliases=aliases,
    )(left, left, right, right, right_next, right_next, valid, lag_weights, lag_weights, *extra)


def per_device(spectra, pair_first, pair_second, pair_count):
    n_w, block_size, n_c, twice = spectra.shape
    bins_count = twice // 2
    owners = lax.axis_size("win")
    block_index = lax.axis_index("pair")
    windows_all = n_w * owners
    chunks = CHUNKS
    width = bins_count // chunks
    halves = spectra[:, : block_size // 2].reshape(n_w, block_size // 2, n_c, 2, chunks, width)
    peers = lax.axis_size("pair")
    cut = peers // 2
    relay = 1 if peers >= 4 else None
    sent = []
    for q in range(chunks):
        piece = halves[:, :, :, :, q]
        if relay is None or q < chunks // 2:
            sent.append(shifted(piece, "pair", -1))
            continue
        direct = lax.ppermute(piece, "pair", [(i, i - 1) for i in range(1, peers) if i != cut])
        hop = lax.ppermute(piece, "pair", [(cut, relay)])
        sent.append(direct + lax.ppermute(hop, "pair", [(relay, cut - 1)]))
    lag_weights = lag_table(bins_count, LAGS, windows_all)
    block_start = block_index * block_size
    first_local = pair_first[0] - block_start
    second_local = pair_second[0] - block_start
    slots = first_local.shape[0]
    slot_index = jnp.arange(slots, dtype=jnp.int32)
    valid = (slot_index < pair_count[0]).astype(jnp.float32)[:, None]

    own_rows = jnp.transpose(spectra, (0, 2, 1, 3)).reshape(n_w * n_c, block_size, twice)
    own_cols = jnp.arange(block_size, dtype=jnp.int32)
    next_cols = jnp.arange(block_size // 2, dtype=jnp.int32) + block_size
    pick_first = (first_local[:, None] == own_cols[None, :]).astype(jnp.bfloat16)
    pick_own = (second_local[:, None] == own_cols[None, :]).astype(jnp.bfloat16)
    pick_next = (second_local[:, None] == next_cols[None, :]).astype(jnp.bfloat16)
    left = jnp.einsum("ps,xsk->xpk", pick_first, own_rows, preferred_element_type=jnp.bfloat16)
    right = jnp.einsum("ps,xsk->xpk", pick_own, own_rows, preferred_element_type=jnp.bfloat16)

    partial = None
    for q in range(chunks):
        next_rows = jnp.transpose(sent[q], (0, 2, 1, 3, 4)).reshape(
            n_w * n_c, block_size // 2, 2 * width
        )
        picks = pick_next
        if partial is not None:
            picks, partial = lax.optimization_barrier((pick_next, partial))
        right_next = jnp.einsum("ps,xsk->xpk", picks, next_rows, preferred_element_type=jnp.bfloat16)
        partial = stacks_of(left, right, right_next, valid, lag_weights, owners, q, chunks, partial)
    partial = jnp.transpose(partial, (1, 0, 2, 3))
    received = lax.all_to_all(partial, "win", 0, 0, tiled=True)
    mine = jnp.sum(received, axis=0)
    return jnp.transpose(mine, (1, 0, 2))


def solution(mesh):
    return jax.shard_map(
        per_device,
        mesh=mesh,
        in_specs=(P("win", "pair", None, None), P("pair", None), P("pair", None), P("pair")),
        out_specs=P(("pair", "win"), None, None),
        check_vma=False,
    )
```
